32 devices in a mesh: ctx: 8 (over y, x, core), tp: 4 (over z).
Axes of the slice: x: 2, y: 2, z: 4, core: 2. Of those that a mesh axis runs over, the one named last changes fastest.
Arguments:
- q_in: bfloat16 [1024, 8192], P('ctx', 'tp'), may hold values from -6 to 6
- k_in: bfloat16 [1024, 8192], P('ctx', 'tp'), may hold values from -6 to 6
- v_in: bfloat16 [1024, 8192], P('ctx', 'tp'), may hold values from -6 to 6
- short_filter: float32 [3, 3, 8192], P(None, None, 'tp'), may hold values from -3 to 3
- rate: float32 [8192, 16], P('tp'), may hold values from 9.765625e-05 to 0.05
- residue: float32 [8192, 16], P('tp'), may hold values from -0.3125 to 0.3125
- resid: bfloat16 [1024, 8192], P('ctx', 'tp'), may hold values from -18 to 18, as said below
- gain: float32 [8192], P('tp'), may hold values from 0.5 to 1.5
Outputs:
- normed: bfloat16 [1024, 8192], P('ctx', 'tp')
The draws below stay inside these ranges and needn't reach their ends.
Inputs may be any that keep to these rules, and one draw needn't show every extreme that they name: `resid`: residual stream entries; channel scales differ across the width.
All inputs are finite; a program needn't handle non-finite values.
Results may differ from the reference program's by a relative error of at most 0.0042.
Values may be sent and summed in bfloat16 or wider, within the bound.
No kernel may reach another device: no remote copies, remote signals or barrier semaphores. Data moves between devices by JAX's collectives and lax.ppermute only.
A program may use at most 64 MiB of HBM per device.

```python
import math
import jax
import jax.numpy as jnp
from jax import lax

D = 8192
MODES = 16
SHORT = 3
SEQ = 1024


def draw_resid(key, part):
    ramp = jnp.arange(D, dtype=jnp.float32) / D
    base = jnp.clip(jax.random.normal(key, (SEQ, D), jnp.float32), -6.0, 6.0)
    scale = 1.0 + 2.0 * ramp
    return (base * scale[None, :]).astype(jnp.bfloat16)


def shard_levels(own_key, shape, cuts, smallest, high):
    factor_of, own = 1.0, jax.random.fold_in(own_key, 6)
    for dim, shards_of in cuts:
        heights = jnp.exp(jax.random.uniform(jax.random.fold_in(own, dim), (shards_of,), jnp.float32, smallest / len(cuts), high / len(cuts)))
        factor_of = factor_of * jnp.repeat(heights, shape[dim] // shards_of).reshape([-1 if axis == dim else 1 for axis in range(len(shape))])
    return factor_of


def centred(key, extent, deviation, limit, shards=(), held_as=jnp.bfloat16):
    entries = deviation * jax.random.normal(key, extent, jnp.float32)
    if shards:
        entries = entries * shard_levels(key, extent, shards, -0.22, 0.18)
    return jnp.clip(entries, -limit, limit).astype(held_as)


def setup_inputs(seed: int = 0) -> dict:
    key_list = jax.random.split(jax.random.key(seed), 9)
    q_in = centred(key_list[0], (SEQ, D), 1.0, 6.0, ((0, 8), (1, 4)))
    k_in = centred(key_list[1], (SEQ, D), 1.0, 6.0, ((0, 8), (1, 4)))
    v_in = centred(key_list[2], (SEQ, D), 1.0, 6.0, ((0, 8), (1, 4)))
    short_filter = centred(key_list[3], (3, SHORT, D), 0.5, 3.0, ((2, 4),), jnp.float32)
    rate = jnp.clip(jnp.exp(math.log(0.05) - 6.2383246 * jax.random.uniform(key_list[4], (D, MODES), jnp.float32) ** shard_levels(key_list[4], (D, MODES), ((0, 4),), -0.2, 0.2)), 9.765625145519152e-05, 0.05)
    residue = centred(key_list[5], (D, MODES), 0.02, 0.3125, ((0, 4),), jnp.float32)
    resid = draw_resid(jax.random.fold_in(key_list[8], 71), 0)
    gain = jnp.clip(1.0 + 0.1 * jax.random.normal(key_list[7], (D,), jnp.float32), 0.5, 1.5)
    return {"q_in": q_in, "k_in": k_in, "v_in": v_in, "short_filter": short_filter, "rate": rate, "residue": residue, "resid": resid, "gain": gain}


def short_conv(stream, taps):
    values = stream.astype(jnp.float32)
    out = taps[0] * values
    for j in range(1, SHORT):
        shifted = jnp.concatenate([jnp.zeros((j, values.shape[1]), jnp.float32), values[:-j]], axis=0)
        out = out + taps[j] * shifted
    return out

def long_conv(gated, rate, residue):
    length = gated.shape[0]
    group = min(256, D)
    times = jnp.arange(length, dtype=jnp.int32).astype(jnp.float32)

    def one_group(index):
        start = (index * group).astype(jnp.int32)
        columns = lax.dynamic_slice_in_dim(gated, start, group, 1).astype(jnp.float32).T
        rates = lax.dynamic_slice_in_dim(rate, start, group, 0)
        weights = lax.dynamic_slice_in_dim(residue, start, group, 0)
        filt = jnp.zeros((group, length), jnp.float32)
        for m in range(MODES):
            filt = filt + weights[:, m:m + 1] * jnp.exp(-rates[:, m:m + 1] * times[None, :])
        spectrum = jnp.fft.rfft(columns, n=2 * length, axis=1) * jnp.fft.rfft(filt, n=2 * length, axis=1)
        return jnp.fft.irfft(spectrum, n=2 * length, axis=1)[:, :length]
    pieces = lax.map(one_group, jnp.arange(D // group, dtype=jnp.int32))
    return pieces.reshape(D, length).T

def reference(q_in, k_in, v_in, short_filter, rate, residue, resid, gain):
    q_feat = short_conv(q_in, short_filter[0])
    k_feat = short_conv(k_in, short_filter[1])
    v_feat = short_conv(v_in, short_filter[2])
    gated = lax.optimization_barrier((k_feat * v_feat).astype(jnp.bfloat16))
    mixed = long_conv(gated, rate, residue)
    stream = resid.astype(jnp.float32) + q_feat * mixed
    scale = lax.rsqrt(lax.optimization_barrier(jnp.sum(stream * stream, axis=1, keepdims=True)) / D + 1e-05)
    return (stream * scale * gain[None, :]).astype(jnp.bfloat16)
```

```python
import jax
import jax.numpy as jnp
from jax import lax
from jax.sharding import PartitionSpec as P

D = 8192


def from_behind(block, axis, distance):
    devices = range(lax.axis_size(axis))
    route = [(i - distance, i) for i in devices if i - distance in devices]
    return lax.ppermute(block, axis, route)


def scan_in(ending, rate, rows, axis):
    count = lax.axis_size(axis)
    if count == 1:
        return jnp.zeros_like(ending)
    incoming = from_behind(ending, axis, 1)
    if count > 2:
        incoming = incoming + jnp.exp(-rate * rows) * from_behind(ending, axis, 2)
    shift = 2
    while shift < count:
        incoming = incoming + jnp.exp(-rate * (rows * shift)) * from_behind(incoming, axis, shift)
        shift *= 2
    return incoming


def butterfly_sum(value, axis):
    count = lax.axis_size(axis)
    assert count & (count - 1) == 0
    step = 1
    while step < count:
        value = value + lax.ppermute(value, axis, [(i, i ^ step) for i in range(count)])
        step *= 2
    return value


def per_device(q_in, k_in, v_in, short_filter, rate, residue, resid, gain):
    rows, width = q_in.shape
    taps = short_filter.shape[1]
    stacked = jnp.stack([q_in, k_in, v_in])
    tail = stacked[:, rows - (taps - 1) :, :]
    before = from_behind(tail, "ctx", 1)
    padded = jnp.concatenate([before, stacked], axis=1).astype(jnp.float32)
    feats = short_filter[:, 0, None, :] * padded[:, taps - 1 :, :]
    for j in range(1, taps):
        feats = (
            feats + short_filter[:, j, None, :] * padded[:, taps - 1 - j : taps - 1 - j + rows, :]
        )
    q_feat = feats[0]
    gated = (feats[1] * feats[2]).astype(jnp.bfloat16)
    values = lax.optimization_barrier(gated).astype(jnp.float32)
    block = min(128, rows)
    blocks = values.reshape(rows // block, block, width)
    offsets = jnp.arange(block, dtype=jnp.int32).astype(jnp.float32)
    grow = jnp.exp(rate[None, :, :] * offsets[:, None, None])
    fade = jnp.exp(-rate[None, :, :] * offsets[:, None, None])
    enter = jnp.exp(-rate[None, :, :] * (offsets[:, None, None] + 1.0))
    last_fade = jnp.exp(-rate * (block - 1))
    block_decay = jnp.exp(-rate * block)

    def end_step(state, piece):
        summed = jnp.einsum("sc,scm->cm", piece, grow)
        return (state * block_decay + last_fade * summed, None)

    zeros = jnp.zeros(rate.shape, jnp.float32)
    ending, unused = lax.scan(end_step, zeros, blocks)
    incoming = scan_in(ending, rate, rows, "ctx")

    def main_step(state, piece):
        running = jnp.cumsum(piece[:, :, None] * grow, axis=0) * fade
        states = running + enter * state[None, :, :]
        return (states[-1], jnp.sum(states * residue[None, :, :], axis=2))

    unused_state, outputs = lax.scan(main_step, incoming, blocks)
    mixed = outputs.reshape(rows, width)
    stream = resid.astype(jnp.float32) + q_feat * mixed
    squares = butterfly_sum(jnp.sum(stream * stream, axis=1), "tp")
    scale = lax.rsqrt(squares / D + 1e-05)
    return (stream * scale[:, None] * gain[None, :]).astype(jnp.bfloat16)


def solution(mesh):
    in_specs = (
        P("ctx", "tp"),
        P("ctx", "tp"),
        P("ctx", "tp"),
        P(None, None, "tp"),
        P("tp", None),
        P("tp", None),
        P("ctx", "tp"),
        P("tp"),
    )
    out_specs = P("ctx", "tp")
    return jax.shard_map(
        per_device, mesh=mesh, in_specs=in_specs, out_specs=out_specs, check_vma=False
    )
```

```python
import jax
import jax.numpy as jnp
from jax import lax
from jax.sharding import PartitionSpec as P

D = 8192


def from_behind(block, axis, distance):
    devices = range(lax.axis_size(axis))
    route = [(i - distance, i) for i in devices if i - distance in devices]
    return lax.ppermute(block, axis, route)


def scan_in(ending, rate, rows, axis, cover):
    count = lax.axis_size(axis)
    radix = min(count, 8)
    arrived = [from_behind(ending, axis, shift) for shift in range(1, radix)]
    arrived, covered = lax.optimization_barrier((arrived, cover()))
    incoming = jnp.zeros_like(ending)
    for shift in range(1, radix):
        incoming = incoming + jnp.exp(-rate * (rows * (shift - 1))) * arrived[shift - 1]
    span = radix - 1
    while span < count - 1:
        incoming = incoming + jnp.exp(-rate * (rows * span)) * from_behind(incoming, axis, span)
        span *= 2
    return incoming, covered


def butterfly_sum(value, axis):
    count = lax.axis_size(axis)
    assert count & (count - 1) == 0
    step = 1
    while step < count:
        value = value + lax.ppermute(value, axis, [(i, i ^ step) for i in range(count)])
        step *= 2
    return value


def per_device(q_in, k_in, v_in, short_filter, rate, residue, resid, gain):
    rows, width = q_in.shape
    taps = short_filter.shape[1]
    stacked = jnp.stack([q_in, k_in, v_in])
    tail = stacked[:, rows - (taps - 1) :, :]
    before = from_behind(tail, "ctx", 1)
    padded = jnp.concatenate([before, stacked], axis=1).astype(jnp.float32)
    feats = short_filter[:, 0, None, :] * padded[:, taps - 1 :, :]
    for j in range(1, taps):
        feats = (
            feats + short_filter[:, j, None, :] * padded[:, taps - 1 - j : taps - 1 - j + rows, :]
        )
    q_feat = feats[0]
    gated = (feats[1] * feats[2]).astype(jnp.bfloat16)
    values = lax.optimization_barrier(gated).astype(jnp.float32)
    block = min(128, rows)
    blocks = values.reshape(rows // block, block, width)
    offsets = jnp.arange(block, dtype=jnp.int32).astype(jnp.float32)
    grow = jnp.exp(rate[None, :, :] * offsets[:, None, None])
    fade = jnp.exp(-rate[None, :, :] * offsets[:, None, None])
    enter = jnp.exp(-rate[None, :, :] * (offsets[:, None, None] + 1.0))
    last_fade = jnp.exp(-rate * (block - 1))
    block_decay = jnp.exp(-rate * block)

    def end_step(state, piece):
        summed = jnp.einsum("sc,scm->cm", piece, grow)
        return (state * block_decay + last_fade * summed, None)

    zeros = jnp.zeros(rate.shape, jnp.float32)
    ending, unused = lax.scan(end_step, zeros, blocks)

    def main_step(state, piece):
        running = jnp.cumsum(piece[:, :, None] * grow, axis=0) * fade
        states = running + enter * state[None, :, :]
        return (states[-1], jnp.sum(states * residue[None, :, :], axis=2))

    def local():
        if rows == block:
            return main_step(zeros, values)[1]
        return lax.scan(main_step, zeros, blocks)[1].reshape(rows, width)

    incoming, outputs = scan_in(ending, rate, rows, "ctx", local)
    times = jnp.arange(rows, dtype=jnp.int32).astype(jnp.float32) + 1.0
    weights = residue * incoming
    mixed_in = jnp.sum(jnp.exp(-rate[None, :, :] * times[:, None, None]) * weights[None, :, :], axis=2)
    mixed = outputs + mixed_in
    stream = resid.astype(jnp.float32) + q_feat * mixed
    squares = butterfly_sum(jnp.sum(stream * stream, axis=1), "tp")
    scale = lax.rsqrt(squares / D + 1e-05)
    return (stream * scale[:, None] * gain[None, :]).astype(jnp.bfloat16)


def solution(mesh):
    in_specs = (
        P("ctx", "tp"),
        P("ctx", "tp"),
        P("ctx", "tp"),
        P(None, None, "tp"),
        P("tp", None),
        P("tp", None),
        P("ctx", "tp"),
        P("tp"),
    )
    out_specs = P("ctx", "tp")
    step = jax.shard_map(
        per_device, mesh=mesh, in_specs=in_specs, out_specs=out_specs, check_vma=False
    )
    return step
```

```python
import jax
import jax.numpy as jnp
from jax import lax
from jax.sharding import PartitionSpec as P

D = 8192


def from_behind(block, axis, distance):
    devices = range(lax.axis_size(axis))
    route = [(i - distance, i) for i in devices if i - distance in devices]
    return lax.ppermute(block, axis, route)


def scan_in(ending, rate, rows, axis, cover):
    count = lax.axis_size(axis)
    radix = min(count, 8)
    arrived = [from_behind(ending, axis, shift) for shift in range(1, radix)]
    arrived, covered = lax.optimization_barrier((arrived, cover()))
    incoming = jnp.zeros_like(ending)
    for shift in range(1, radix):
        incoming = incoming + jnp.exp(-rate * (rows * (shift - 1))) * arrived[shift - 1]
    span = radix - 1
    while span < count - 1:
        incoming = incoming + jnp.exp(-rate * (rows * span)) * from_behind(incoming, axis, span)
        span *= 2
    return incoming, covered


def butterfly_sum(value, axis):
    count = lax.axis_size(axis)
    assert count & (count - 1) == 0
    step = 1
    while step < count:
        value = value + lax.ppermute(value, axis, [(i, i ^ step) for i in range(count)])
        step *= 2
    return value


def per_device(q_in, k_in, v_in, short_filter, rate, residue, resid, gain):
    rows, width = q_in.shape
    taps = short_filter.shape[1]
    stacked = jnp.stack([q_in, k_in, v_in])
    tail = stacked[:, rows - (taps - 1) :, :]
    before = from_behind(tail, "ctx", 1)
    padded = jnp.concatenate([before, stacked], axis=1).astype(jnp.float32)
    feats = short_filter[:, 0, None, :] * padded[:, taps - 1 :, :]
    for j in range(1, taps):
        feats = (
            feats + short_filter[:, j, None, :] * padded[:, taps - 1 - j : taps - 1 - j + rows, :]
        )
    q_feat = feats[0]
    gated = (feats[1] * feats[2]).astype(jnp.bfloat16)
    values = lax.optimization_barrier(gated).astype(jnp.float32)
    block = min(128, rows)
    blocks = values.reshape(rows // block, block, width)
    offsets = jnp.arange(block, dtype=jnp.int32).astype(jnp.float32)
    grow = jnp.exp(rate[None, :, :] * offsets[:, None, None])
    fade = jnp.exp(-rate[None, :, :] * offsets[:, None, None])
    enter = jnp.exp(-rate[None, :, :] * (offsets[:, None, None] + 1.0))
    last_fade = jnp.exp(-rate * (block - 1))
    block_decay = jnp.exp(-rate * block)

    def end_step(state, piece):
        summed = jnp.einsum("sc,scm->cm", piece, grow)
        return (state * block_decay + last_fade * summed, None)

    zeros = jnp.zeros(rate.shape, jnp.float32)
    lower = (offsets[:, None] >= offsets[None, :]).astype(jnp.float32)

    def cumulative(terms):
        return jnp.einsum("ts,scm->tcm", lower, terms, precision=lax.Precision.HIGHEST)

    ending, unused = lax.scan(end_step, zeros, blocks)

    def main_step(state, piece):
        running = cumulative(piece[:, :, None] * grow) * fade
        states = running + enter * state[None, :, :]
        return (states[-1], jnp.sum(states * residue[None, :, :], axis=2))

    def local():
        if rows == block:
            running = cumulative(values[:, :, None] * grow) * fade
            return jnp.sum(running * residue[None, :, :], axis=2)
        return lax.scan(main_step, zeros, blocks)[1].reshape(rows, width)

    incoming, outputs = scan_in(ending, rate, rows, "ctx", local)
    times = jnp.arange(rows, dtype=jnp.int32).astype(jnp.float32) + 1.0
    weights = residue * incoming
    mixed_in = jnp.sum(jnp.exp(-rate[None, :, :] * times[:, None, None]) * weights[None, :, :], axis=2)
    mixed = outputs + mixed_in
    stream = resid.astype(jnp.float32) + q_feat * mixed
    squares = butterfly_sum(jnp.sum(stream * stream, axis=1), "tp")
    scale = lax.rsqrt(squares / D + 1e-05)
    return (stream * scale[:, None] * gain[None, :]).astype(jnp.bfloat16)


def solution(mesh):
    in_specs = (
        P("ctx", "tp"),
        P("ctx", "tp"),
        P("ctx", "tp"),
        P(None, None, "tp"),
        P("tp", None),
        P("tp", None),
        P("ctx", "tp"),
        P("tp"),
    )
    out_specs = P("ctx", "tp")
    step = jax.shard_map(
        per_device, mesh=mesh, in_specs=in_specs, out_specs=out_specs, check_vma=False
    )
    return step
```

```python
import jax
import jax.numpy as jnp
from jax import lax
from jax.sharding import PartitionSpec as P

D = 8192


def from_behind(block, axis, distance):
    devices = range(lax.axis_size(axis))
    route = [(i - distance, i) for i in devices if i - distance in devices]
    return lax.ppermute(block, axis, route)


def scan_in(ending, rate, rows, axis, cover):
    count = lax.axis_size(axis)
    radix = min(count, 8)
    arrived = [from_behind(ending, axis, shift) for shift in range(1, radix)]
    arrived, covered = lax.optimization_barrier((arrived, cover()))
    incoming = jnp.zeros_like(ending)
    for shift in range(1, radix):
        incoming = incoming + jnp.exp(-rate * (rows * (shift - 1))) * arrived[shift - 1]
    span = radix - 1
    while span < count - 1:
        incoming = incoming + jnp.exp(-rate * (rows * span)) * from_behind(incoming, axis, span)
        span *= 2
    return incoming, covered


def butterfly_sum(value, axis):
    count = lax.axis_size(axis)
    assert count & (count - 1) == 0
    step = 1
    while step < count:
        value = value + lax.ppermute(value, axis, [(i, i ^ step) for i in range(count)])
        step *= 2
    return value


def per_device(q_in, k_in, v_in, short_filter, rate, residue, resid, gain):
    rows, width = q_in.shape
    taps = short_filter.shape[1]
    stacked = jnp.stack([q_in, k_in, v_in])
    tail = stacked[:, rows - (taps - 1) :, :]
    before = from_behind(tail, "ctx", 1)
    padded = jnp.concatenate([before, stacked], axis=1).astype(jnp.float32)
    feats = short_filter[:, 0, None, :] * padded[:, taps - 1 :, :]
    for j in range(1, taps):
        feats = (
            feats + short_filter[:, j, None, :] * padded[:, taps - 1 - j : taps - 1 - j + rows, :]
        )
    q_feat = feats[0]
    gated = (feats[1] * feats[2]).astype(jnp.bfloat16)
    values = lax.optimization_barrier(gated).astype(jnp.float32)
    block = min(128, rows)
    blocks = values.reshape(rows // block, block, width)
    offsets = jnp.arange(block, dtype=jnp.int32).astype(jnp.float32)
    grow = jnp.exp(rate[None, :, :] * offsets[:, None, None])
    fade = jnp.exp(-rate[None, :, :] * offsets[:, None, None])
    enter = jnp.exp(-rate[None, :, :] * (offsets[:, None, None] + 1.0))
    last_fade = jnp.exp(-rate * (block - 1))
    block_decay = jnp.exp(-rate * block)

    def end_step(state, piece):
        summed = jnp.einsum("sc,scm->cm", piece, grow)
        return (state * block_decay + last_fade * summed, None)

    zeros = jnp.zeros(rate.shape, jnp.float32)
    ending, unused = lax.scan(end_step, zeros, blocks)

    def main_step(state, piece):
        running = jnp.cumsum(piece[:, :, None] * grow, axis=0) * fade
        states = running + enter * state[None, :, :]
        return (states[-1], jnp.sum(states * residue[None, :, :], axis=2))

    def local():
        if rows == block:
            running = jnp.cumsum(values[:, :, None] * grow, axis=0) * fade
            return jnp.sum(running * residue[None, :, :], axis=2)
        return lax.scan(main_step, zeros, blocks)[1].reshape(rows, width)

    incoming, outputs = scan_in(ending, rate, rows, "ctx", local)
    times = jnp.arange(rows, dtype=jnp.int32).astype(jnp.float32) + 1.0
    weights = residue * incoming
    mixed_in = jnp.sum(jnp.exp(-rate[None, :, :] * times[:, None, None]) * weights[None, :, :], axis=2)
    mixed = outputs + mixed_in
    stream = resid.astype(jnp.float32) + q_feat * mixed
    squares = butterfly_sum(jnp.sum(stream * stream, axis=1), "tp")
    scale = lax.rsqrt(squares / D + 1e-05)
    return (stream * scale[:, None] * gain[None, :]).astype(jnp.bfloat16)


def solution(mesh):
    in_specs = (
        P("ctx", "tp"),
        P("ctx", "tp"),
        P("ctx", "tp"),
        P(None, None, "tp"),
        P("tp", None),
        P("tp", None),
        P("ctx", "tp"),
        P("tp"),
    )
    out_specs = P("ctx", "tp")
    step = jax.shard_map(
        per_device, mesh=mesh, in_specs=in_specs, out_specs=out_specs, check_vma=False
    )
    return step
```

```python
import jax
import jax.numpy as jnp
from jax import lax
from jax.sharding import PartitionSpec as P

D = 8192


def from_behind(block, axis, distance):
    devices = range(lax.axis_size(axis))
    route = [(i - distance, i) for i in devices if i - distance in devices]
    return lax.ppermute(block, axis, route)


def scan_in(ending, rate, rows, axis, cover):
    count = lax.axis_size(axis)
    radix = min(count, 8)
    arrived = [from_behind(ending, axis, shift) for shift in range(1, radix)]
    arrived, covered = lax.optimization_barrier((arrived, cover()))
    incoming = jnp.zeros_like(ending)
    for shift in range(1, radix):
        incoming = incoming + jnp.exp(-rate * (rows * (shift - 1))) * arrived[shift - 1]
    span = radix - 1
    while span < count - 1:
        incoming = incoming + jnp.exp(-rate * (rows * span)) * from_behind(incoming, axis, span)
        span *= 2
    return incoming, covered


def butterfly_sum(value, axis):
    count = lax.axis_size(axis)
    assert count & (count - 1) == 0
    step = 1
    while step < count:
        value = value + lax.ppermute(value, axis, [(i, i ^ step) for i in range(count)])
        step *= 2
    return value


def per_device(q_in, k_in, v_in, short_filter, rate, residue, resid, gain):
    rows, width = q_in.shape
    taps = short_filter.shape[1]
    stacked = jnp.stack([q_in, k_in, v_in])
    tail = stacked[:, rows - (taps - 1) :, :]
    before = from_behind(tail, "ctx", 1)
    padded = jnp.concatenate([before, stacked], axis=1).astype(jnp.float32)
    feats = short_filter[:, 0, None, :] * padded[:, taps - 1 :, :]
    for j in range(1, taps):
        feats = (
            feats + short_filter[:, j, None, :] * padded[:, taps - 1 - j : taps - 1 - j + rows, :]
        )
    q_feat = feats[0]
    gated = (feats[1] * feats[2]).astype(jnp.bfloat16)
    values = lax.optimization_barrier(gated).astype(jnp.float32)
    block = min(128, rows)
    blocks = values.reshape(rows // block, block, width)
    decay = rate.T
    weight = residue.T
    offsets = jnp.arange(block, dtype=jnp.int32).astype(jnp.float32)
    grow = jnp.exp(decay[:, None, :] * offsets[None, :, None])
    fade = jnp.exp(-decay[:, None, :] * offsets[None, :, None])
    enter = jnp.exp(-decay[:, None, :] * (offsets[None, :, None] + 1.0))
    last_fade = jnp.exp(-decay * (block - 1))
    block_decay = jnp.exp(-decay * block)

    def end_step(state, piece):
        summed = jnp.einsum("sc,msc->mc", piece, grow)
        return (state * block_decay + last_fade * summed, None)

    zeros = jnp.zeros(decay.shape, jnp.float32)
    ending, unused = lax.scan(end_step, zeros, blocks)

    def main_step(state, piece):
        running = jnp.cumsum(piece[None, :, :] * grow, axis=1) * fade
        states = running + enter * state[:, None, :]
        return (states[:, -1, :], jnp.sum(states * weight[:, None, :], axis=0))

    def local():
        if rows == block:
            running = jnp.cumsum(values[None, :, :] * grow, axis=1) * fade
            return jnp.sum(running * weight[:, None, :], axis=0)
        return lax.scan(main_step, zeros, blocks)[1].reshape(rows, width)

    incoming, outputs = scan_in(ending, decay, rows, "ctx", local)
    times = jnp.arange(rows, dtype=jnp.int32).astype(jnp.float32) + 1.0
    weights = weight * incoming
    mixed_in = jnp.sum(jnp.exp(-decay[:, None, :] * times[None, :, None]) * weights[:, None, :], axis=0)
    mixed = outputs + mixed_in
    stream = resid.astype(jnp.float32) + q_feat * mixed
    squares = butterfly_sum(jnp.sum(stream * stream, axis=1), "tp")
    scale = lax.rsqrt(squares / D + 1e-05)
    return (stream * scale[:, None] * gain[None, :]).astype(jnp.bfloat16)


def solution(mesh):
    in_specs = (
        P("ctx", "tp"),
        P("ctx", "tp"),
        P("ctx", "tp"),
        P(None, None, "tp"),
        P("tp", None),
        P("tp", None),
        P("ctx", "tp"),
        P("tp"),
    )
    out_specs = P("ctx", "tp")
    step = jax.shard_map(
        per_device, mesh=mesh, in_specs=in_specs, out_specs=out_specs, check_vma=False
    )
    return step
```

```python
import jax
import jax.numpy as jnp
from jax import lax
from jax.sharding import PartitionSpec as P
from jax.experimental import pallas as pl
from jax.experimental.pallas import tpu as pltpu

D = 8192


def from_behind(block, axis, distance):
    devices = range(lax.axis_size(axis))
    route = [(i - distance, i) for i in devices if i - distance in devices]
    return lax.ppermute(block, axis, route)


def scan_in(ending, rate, rows, axis, cover):
    count = lax.axis_size(axis)
    radix = min(count, 8)
    arrived = [from_behind(ending, axis, shift) for shift in range(1, radix)]
    arrived, covered = lax.optimization_barrier((arrived, cover()))
    incoming = jnp.zeros_like(ending)
    for shift in range(1, radix):
        incoming = incoming + jnp.exp(-rate * (rows * (shift - 1))) * arrived[shift - 1]
    span = radix - 1
    while span < count - 1:
        incoming = incoming + jnp.exp(-rate * (rows * span)) * from_behind(incoming, axis, span)
        span *= 2
    return incoming, covered


def butterfly_sum(value, axis):
    count = lax.axis_size(axis)
    assert count & (count - 1) == 0
    step = 1
    while step < count:
        value = value + lax.ppermute(value, axis, [(i, i ^ step) for i in range(count)])
        step *= 2
    return value


def front_kernel(q_ref, k_ref, v_ref, halo_ref, taps_ref, coarse_ref, fine_ref, qf_ref, g_ref, end_ref, pad_ref):
    rows = q_ref.shape[0]
    lead = pad_ref.shape[1] - rows
    feats = []
    for i, ref in enumerate((q_ref, k_ref, v_ref)):
        pad_ref[i, lead:, :] = ref[...].astype(jnp.float32)
        pad_ref[i, lead - 2 : lead, :] = halo_ref[i].astype(jnp.float32)
        acc = taps_ref[i, 0:1, :] * pad_ref[i, lead:, :]
        for j in (1, 2):
            acc = acc + taps_ref[i, j : j + 1, :] * pad_ref[i, lead - j : lead - j + rows, :]
        feats.append(acc)
    qf_ref[...] = feats[0]
    gated = (feats[1] * feats[2]).astype(jnp.bfloat16).astype(jnp.float32)
    g_ref[...] = gated
    chunks = rows // 8

    def mode(m, carry):
        weights = coarse_ref[m]
        inner = weights[0:1, :] * gated[0:8, :]
        for u in range(1, chunks):
            inner = inner + weights[u : u + 1, :] * gated[8 * u : 8 * u + 8, :]
        end_ref[pl.ds(m, 1), :] = jnp.sum(inner * fine_ref[m], axis=0, keepdims=True)
        return carry

    lax.fori_loop(0, coarse_ref.shape[0], mode, 0)


def front(q_in, k_in, v_in, before, short_filter, decay):
    rows, width = q_in.shape
    modes = decay.shape[0]
    chunks = rows // 8
    coarse = jnp.exp(-decay[:, None, :] * (8.0 * (chunks - 1 - jnp.arange(chunks, dtype=jnp.float32)))[None, :, None])
    fine = jnp.exp(-decay[:, None, :] * (7.0 - jnp.arange(8, dtype=jnp.float32))[None, :, None])
    vmem = pl.BlockSpec(memory_space=pltpu.VMEM)
    return pl.pallas_call(
        front_kernel,
        out_shape=(
            jax.ShapeDtypeStruct((rows, width), jnp.float32),
            jax.ShapeDtypeStruct((rows, width), jnp.float32),
            jax.ShapeDtypeStruct((modes, width), jnp.float32),
        ),
        in_specs=[vmem] * 7,
        out_specs=(vmem, vmem, vmem),
        scratch_shapes=[pltpu.VMEM((3, rows + 8, width), jnp.float32)],
        compiler_params=pltpu.CompilerParams(vmem_limit_bytes=48 * 1024 * 1024),
        cost_estimate=pl.CostEstimate(
            flops=2 * rows * width * (9 + 2 * modes), transcendentals=0, bytes_accessed=rows * width * 14
        ),
    )(q_in, k_in, v_in, before, short_filter, coarse, fine)


def per_device(q_in, k_in, v_in, short_filter, rate, residue, resid, gain):
    rows, width = q_in.shape
    taps = short_filter.shape[1]
    stacked = jnp.stack([q_in, k_in, v_in])
    tail = stacked[:, rows - (taps - 1) :, :]
    before = from_behind(tail, "ctx", 1)
    decay = rate.T
    weight = residue.T
    q_feat, values, ending = front(q_in, k_in, v_in, before, short_filter, decay)
    block = min(128, rows)
    blocks = values.reshape(rows // block, block, width)
    offsets = jnp.arange(block, dtype=jnp.int32).astype(jnp.float32)
    grow = jnp.exp(decay[:, None, :] * offsets[None, :, None])
    fade = jnp.exp(-decay[:, None, :] * offsets[None, :, None])
    enter = jnp.exp(-decay[:, None, :] * (offsets[None, :, None] + 1.0))
    zeros = jnp.zeros(decay.shape, jnp.float32)

    def main_step(state, piece):
        running = jnp.cumsum(piece[None, :, :] * grow, axis=1) * fade
        states = running + enter * state[:, None, :]
        return (states[:, -1, :], jnp.sum(states * weight[:, None, :], axis=0))

    def local():
        if rows == block:
            running = jnp.cumsum(values[None, :, :] * grow, axis=1) * fade
            return jnp.sum(running * weight[:, None, :], axis=0)
        return lax.scan(main_step, zeros, blocks)[1].reshape(rows, width)

    incoming, outputs = scan_in(ending, decay, rows, "ctx", local)
    times = jnp.arange(rows, dtype=jnp.int32).astype(jnp.float32) + 1.0
    weights = weight * incoming
    mixed_in = jnp.sum(jnp.exp(-decay[:, None, :] * times[None, :, None]) * weights[:, None, :], axis=0)
    mixed = outputs + mixed_in
    stream = resid.astype(jnp.float32) + q_feat * mixed
    squares = butterfly_sum(jnp.sum(stream * stream, axis=1), "tp")
    scale = lax.rsqrt(squares / D + 1e-05)
    return (stream * scale[:, None] * gain[None, :]).astype(jnp.bfloat16)


def solution(mesh):
    in_specs = (
        P("ctx", "tp"),
        P("ctx", "tp"),
        P("ctx", "tp"),
        P(None, None, "tp"),
        P("tp", None),
        P("tp", None),
        P("ctx", "tp"),
        P("tp"),
    )
    out_specs = P("ctx", "tp")
    step = jax.shard_map(
        per_device, mesh=mesh, in_specs=in_specs, out_specs=out_specs, check_vma=False
    )
    return step
```

```python
import jax
import jax.numpy as jnp
from jax import lax
from jax.sharding import PartitionSpec as P
from jax.experimental import pallas as pl
from jax.experimental.pallas import tpu as pltpu

D = 8192


def from_behind(block, axis, distance):
    devices = range(lax.axis_size(axis))
    route = [(i - distance, i) for i in devices if i - distance in devices]
    return lax.ppermute(block, axis, route)


def scan_in(ending, rate, rows, axis, cover):
    count = lax.axis_size(axis)
    radix = min(count, 8)
    ending, covered = lax.optimization_barrier((ending, cover()))
    arrived = [from_behind(ending, axis, shift) for shift in range(1, radix)]
    incoming = jnp.zeros_like(ending)
    for shift in range(1, radix):
        incoming = incoming + jnp.exp(-rate * (rows * (shift - 1))) * arrived[shift - 1]
    span = radix - 1
    while span < count - 1:
        incoming = incoming + jnp.exp(-rate * (rows * span)) * from_behind(incoming, axis, span)
        span *= 2
    return incoming, covered


def butterfly_sum(value, axis):
    count = lax.axis_size(axis)
    assert count & (count - 1) == 0
    step = 1
    while step < count:
        value = value + lax.ppermute(value, axis, [(i, i ^ step) for i in range(count)])
        step *= 2
    return value


def front_kernel(q_ref, k_ref, v_ref, halo_ref, taps_ref, coarse_ref, fine_ref, qf_ref, g_ref, end_ref, pad_ref):
    rows = q_ref.shape[0]
    lead = pad_ref.shape[1] - rows
    feats = []
    for i, ref in enumerate((q_ref, k_ref, v_ref)):
        pad_ref[i, lead:, :] = ref[...].astype(jnp.float32)
        pad_ref[i, lead - 2 : lead, :] = halo_ref[i].astype(jnp.float32)
        acc = taps_ref[i, 0:1, :] * pad_ref[i, lead:, :]
        for j in (1, 2):
            acc = acc + taps_ref[i, j : j + 1, :] * pad_ref[i, lead - j : lead - j + rows, :]
        feats.append(acc)
    qf_ref[...] = feats[0]
    gated = (feats[1] * feats[2]).astype(jnp.bfloat16).astype(jnp.float32)
    g_ref[...] = gated
    chunks = rows // 8

    def mode(m, carry):
        weights = coarse_ref[m]
        inner = weights[0:1, :] * gated[0:8, :]
        for u in range(1, chunks):
            inner = inner + weights[u : u + 1, :] * gated[8 * u : 8 * u + 8, :]
        end_ref[pl.ds(m, 1), :] = jnp.sum(inner * fine_ref[m], axis=0, keepdims=True)
        return carry

    lax.fori_loop(0, coarse_ref.shape[0], mode, 0)


def front(q_in, k_in, v_in, before, short_filter, decay):
    rows, width = q_in.shape
    modes = decay.shape[0]
    chunks = rows // 8
    coarse = jnp.exp(-decay[:, None, :] * (8.0 * (chunks - 1 - jnp.arange(chunks, dtype=jnp.float32)))[None, :, None])
    fine = jnp.exp(-decay[:, None, :] * (7.0 - jnp.arange(8, dtype=jnp.float32))[None, :, None])
    vmem = pl.BlockSpec(memory_space=pltpu.VMEM)
    return pl.pallas_call(
        front_kernel,
        out_shape=(
            jax.ShapeDtypeStruct((rows, width), jnp.float32),
            jax.ShapeDtypeStruct((rows, width), jnp.float32),
            jax.ShapeDtypeStruct((modes, width), jnp.float32),
        ),
        in_specs=[vmem] * 7,
        out_specs=(vmem, vmem, vmem),
        scratch_shapes=[pltpu.VMEM((3, rows + 8, width), jnp.float32)],
        compiler_params=pltpu.CompilerParams(vmem_limit_bytes=48 * 1024 * 1024),
        cost_estimate=pl.CostEstimate(
            flops=2 * rows * width * (9 + 2 * modes), transcendentals=0, bytes_accessed=rows * width * 14
        ),
    )(q_in, k_in, v_in, before, short_filter, coarse, fine)


def per_device(q_in, k_in, v_in, short_filter, rate, residue, resid, gain):
    rows, width = q_in.shape
    taps = short_filter.shape[1]
    stacked = jnp.stack([q_in, k_in, v_in])
    tail = stacked[:, rows - (taps - 1) :, :]
    before = from_behind(tail, "ctx", 1)
    decay = rate.T
    weight = residue.T
    q_feat, values, ending = front(q_in, k_in, v_in, before, short_filter, decay)
    block = min(128, rows)
    blocks = values.reshape(rows // block, block, width)
    offsets = jnp.arange(block, dtype=jnp.int32).astype(jnp.float32)
    grow = jnp.exp(decay[:, None, :] * offsets[None, :, None])
    fade = jnp.exp(-decay[:, None, :] * offsets[None, :, None])
    enter = jnp.exp(-decay[:, None, :] * (offsets[None, :, None] + 1.0))
    zeros = jnp.zeros(decay.shape, jnp.float32)

    def main_step(state, piece):
        running = jnp.cumsum(piece[None, :, :] * grow, axis=1) * fade
        states = running + enter * state[:, None, :]
        return (states[:, -1, :], jnp.sum(states * weight[:, None, :], axis=0))

    def local():
        if rows == block:
            running = jnp.cumsum(values[None, :, :] * grow, axis=1) * fade
            return jnp.sum(running * weight[:, None, :], axis=0)
        return lax.scan(main_step, zeros, blocks)[1].reshape(rows, width)

    incoming, outputs = scan_in(ending, decay, rows, "ctx", local)
    times = jnp.arange(rows, dtype=jnp.int32).astype(jnp.float32) + 1.0
    weights = weight * incoming
    mixed_in = jnp.sum(jnp.exp(-decay[:, None, :] * times[None, :, None]) * weights[:, None, :], axis=0)
    mixed = outputs + mixed_in
    stream = resid.astype(jnp.float32) + q_feat * mixed
    squares = butterfly_sum(jnp.sum(stream * stream, axis=1), "tp")
    scale = lax.rsqrt(squares / D + 1e-05)
    return (stream * scale[:, None] * gain[None, :]).astype(jnp.bfloat16)


def solution(mesh):
    in_specs = (
        P("ctx", "tp"),
        P("ctx", "tp"),
        P("ctx", "tp"),
        P(None, None, "tp"),
        P("tp", None),
        P("tp", None),
        P("ctx", "tp"),
        P("tp"),
    )
    out_specs = P("ctx", "tp")
    step = jax.shard_map(
        per_device, mesh=mesh, in_specs=in_specs, out_specs=out_specs, check_vma=False
    )
    return step
```

```python
import jax
import jax.numpy as jnp
from jax import lax
from jax.sharding import PartitionSpec as P
from jax.experimental import pallas as pl
from jax.experimental.pallas import tpu as pltpu

D = 8192


def from_behind(block, axis, distance):
    devices = range(lax.axis_size(axis))
    route = [(i - distance, i) for i in devices if i - distance in devices]
    return lax.ppermute(block, axis, route)


def scan_in(ending, rate, rows, axis, cover):
    count = lax.axis_size(axis)
    radix = min(count, 8)
    arrived = [from_behind(ending, axis, shift) for shift in range(1, radix)]
    arrived, covered = lax.optimization_barrier((arrived, cover()))
    incoming = jnp.zeros_like(ending)
    for shift in range(1, radix):
        incoming = incoming + jnp.exp(-rate * (rows * (shift - 1))) * arrived[shift - 1]
    span = radix - 1
    while span < count - 1:
        incoming = incoming + jnp.exp(-rate * (rows * span)) * from_behind(incoming, axis, span)
        span *= 2
    return incoming, covered


def butterfly_sum(value, axis):
    count = lax.axis_size(axis)
    assert count & (count - 1) == 0
    step = 1
    while step < count:
        value = value + lax.ppermute(value, axis, [(i, i ^ step) for i in range(count)])
        step *= 2
    return value


def front_kernel(q_ref, k_ref, v_ref, halo_ref, taps_ref, coarse_ref, fine_ref, qf_ref, g_ref, end_ref, pad_ref):
    rows = q_ref.shape[0]
    lead = pad_ref.shape[1] - rows
    feats = []
    for i, ref in enumerate((q_ref, k_ref, v_ref)):
        pad_ref[i, lead:, :] = ref[...].astype(jnp.float32)
        pad_ref[i, lead - 2 : lead, :] = halo_ref[i].astype(jnp.float32)
        acc = taps_ref[i, 0:1, :] * pad_ref[i, lead:, :]
        for j in (1, 2):
            acc = acc + taps_ref[i, j : j + 1, :] * pad_ref[i, lead - j : lead - j + rows, :]
        feats.append(acc)
    qf_ref[...] = feats[0]
    gated = (feats[1] * feats[2]).astype(jnp.bfloat16).astype(jnp.float32)
    g_ref[...] = gated
    chunks = rows // 8

    def mode(m, carry):
        weights = coarse_ref[m]
        inner = weights[0:1, :] * gated[0:8, :]
        for u in range(1, chunks):
            inner = inner + weights[u : u + 1, :] * gated[8 * u : 8 * u + 8, :]
        end_ref[pl.ds(m, 1), :] = jnp.sum(inner * fine_ref[m], axis=0, keepdims=True)
        return carry

    lax.fori_loop(0, coarse_ref.shape[0], mode, 0)


def front(q_in, k_in, v_in, before, short_filter, decay):
    rows, width = q_in.shape
    modes = decay.shape[0]
    chunks = rows // 8
    coarse = jnp.exp(-decay[:, None, :] * (8.0 * (chunks - 1 - jnp.arange(chunks, dtype=jnp.float32)))[None, :, None])
    fine = jnp.exp(-decay[:, None, :] * (7.0 - jnp.arange(8, dtype=jnp.float32))[None, :, None])
    vmem = pl.BlockSpec(memory_space=pltpu.VMEM)
    return pl.pallas_call(
        front_kernel,
        out_shape=(
            jax.ShapeDtypeStruct((rows, width), jnp.float32),
            jax.ShapeDtypeStruct((rows, width), jnp.float32),
            jax.ShapeDtypeStruct((modes, width), jnp.float32),
        ),
        in_specs=[vmem] * 7,
        out_specs=(vmem, vmem, vmem),
        scratch_shapes=[pltpu.VMEM((3, rows + 8, width), jnp.float32)],
        compiler_params=pltpu.CompilerParams(vmem_limit_bytes=48 * 1024 * 1024),
        cost_estimate=pl.CostEstimate(
            flops=2 * rows * width * (9 + 2 * modes), transcendentals=0, bytes_accessed=rows * width * 14
        ),
    )(q_in, k_in, v_in, before, short_filter, coarse, fine)


def per_device(q_in, k_in, v_in, short_filter, rate, residue, resid, gain):
    rows, width = q_in.shape
    taps = short_filter.shape[1]
    stacked = jnp.stack([q_in, k_in, v_in])
    tail = stacked[:, rows - (taps - 1) :, :]
    before = from_behind(tail, "ctx", 1)
    decay = rate.T
    weight = residue.T
    q_feat, values, ending = front(q_in, k_in, v_in, before, short_filter, decay)
    block = min(128, rows)
    blocks = values.reshape(rows // block, block, width)
    offsets = jnp.arange(block, dtype=jnp.int32).astype(jnp.float32)
    grow = jnp.exp(decay[:, None, :] * offsets[None, :, None])
    fade = jnp.exp(-decay[:, None, :] * offsets[None, :, None])
    enter = jnp.exp(-decay[:, None, :] * (offsets[None, :, None] + 1.0))
    zeros = jnp.zeros(decay.shape, jnp.float32)

    def main_step(state, piece):
        running = jnp.cumsum(piece[None, :, :] * grow, axis=1) * fade
        states = running + enter * state[:, None, :]
        return (states[:, -1, :], jnp.sum(states * weight[:, None, :], axis=0))

    def local():
        if rows == block:
            running = jnp.cumsum(values[None, :, :] * grow, axis=1) * fade
            return jnp.sum(running * weight[:, None, :], axis=0)
        return lax.scan(main_step, zeros, blocks)[1].reshape(rows, width)

    incoming, outputs = scan_in(ending, decay, rows, "ctx", local)
    times = jnp.arange(rows, dtype=jnp.int32).astype(jnp.float32) + 1.0
    weights = weight * incoming
    mixed_in = outputs
    for m in range(decay.shape[0]):
        mixed_in = mixed_in + jnp.exp(-decay[m][None, :] * times[:, None]) * weights[m][None, :]
    mixed = mixed_in
    stream = resid.astype(jnp.float32) + q_feat * mixed
    squares = butterfly_sum(jnp.sum(stream * stream, axis=1), "tp")
    scale = lax.rsqrt(squares / D + 1e-05)
    return (stream * scale[:, None] * gain[None, :]).astype(jnp.bfloat16)


def solution(mesh):
    in_specs = (
        P("ctx", "tp"),
        P("ctx", "tp"),
        P("ctx", "tp"),
        P(None, None, "tp"),
        P("tp", None),
        P("tp", None),
        P("ctx", "tp"),
        P("tp"),
    )
    out_specs = P("ctx", "tp")
    step = jax.shard_map(
        per_device, mesh=mesh, in_specs=in_specs, out_specs=out_specs, check_vma=False
    )
    return step
```

```python
import jax
import jax.numpy as jnp
from jax import lax
from jax.sharding import PartitionSpec as P
from jax.experimental import pallas as pl
from jax.experimental.pallas import tpu as pltpu

D = 8192


def from_behind(block, axis, distance):
    devices = range(lax.axis_size(axis))
    route = [(i - distance, i) for i in devices if i - distance in devices]
    return lax.ppermute(block, axis, route)


def edge_rows(taps, head, tail):
    first = taps[0] * head[0] + taps[1] * tail[1] + taps[2] * tail[0]
    second = taps[0] * head[1] + taps[1] * head[0] + taps[2] * tail[1]
    return jnp.stack([first, second])


def edge_gated(short_filter, head_k, head_v, tail_k, tail_v):
    keys = edge_rows(short_filter[1], head_k, tail_k)
    values = edge_rows(short_filter[2], head_v, tail_v)
    return (keys * values).astype(jnp.bfloat16).astype(jnp.float32)


def scan_in(payload, modes, short_filter, decay, rows, axis, cover):
    count = lax.axis_size(axis)
    radix = min(count, 8)
    got = {shift: from_behind(payload, axis, shift) for shift in range(1, radix + 1) if shift < count}
    got, covered = lax.optimization_barrier((got, cover()))
    nothing = jnp.zeros_like(payload)
    first_end = jnp.exp(-decay * (rows - 1))
    second_end = jnp.exp(-decay * (rows - 2))

    def block_state(shift):
        piece = got[shift]
        before = got.get(shift + 1, nothing)
        start = modes + 2
        fixed = edge_gated(
            short_filter, piece[start : start + 2], piece[start + 2 : start + 4],
            before[start + 6 : start + 8], before[start + 8 : start + 10],
        )
        change = fixed - piece[modes : modes + 2]
        return piece[:modes] + change[0][None, :] * first_end + change[1][None, :] * second_end

    incoming = jnp.zeros((modes, payload.shape[1]), jnp.float32)
    for shift in range(1, radix):
        incoming = incoming + jnp.exp(-decay * (rows * (shift - 1))) * block_state(shift)
    span = radix - 1
    while span < count - 1:
        incoming = incoming + jnp.exp(-decay * (rows * span)) * from_behind(incoming, axis, span)
        span *= 2
    own_tail = got[1][modes + 6 : modes + 12] if 1 in got else nothing[modes + 6 : modes + 12]
    return incoming, own_tail, covered


def butterfly_sum(value, axis):
    count = lax.axis_size(axis)
    assert count & (count - 1) == 0
    step = 1
    while step < count:
        value = value + lax.ppermute(value, axis, [(i, i ^ step) for i in range(count)])
        step *= 2
    return value


def front_kernel(q_ref, k_ref, v_ref, halo_ref, taps_ref, coarse_ref, fine_ref, qf_ref, g_ref, end_ref, pad_ref):
    rows = q_ref.shape[0]
    lead = pad_ref.shape[1] - rows
    feats = []
    for i, ref in enumerate((q_ref, k_ref, v_ref)):
        pad_ref[i, lead:, :] = ref[...].astype(jnp.float32)
        pad_ref[i, lead - 2 : lead, :] = halo_ref[i].astype(jnp.float32)
        acc = taps_ref[i, 0:1, :] * pad_ref[i, lead:, :]
        for j in (1, 2):
            acc = acc + taps_ref[i, j : j + 1, :] * pad_ref[i, lead - j : lead - j + rows, :]
        feats.append(acc)
    qf_ref[...] = feats[0]
    gated = (feats[1] * feats[2]).astype(jnp.bfloat16).astype(jnp.float32)
    g_ref[...] = gated
    chunks = rows // 8

    def mode(m, carry):
        weights = coarse_ref[m]
        inner = weights[0:1, :] * gated[0:8, :]
        for u in range(1, chunks):
            inner = inner + weights[u : u + 1, :] * gated[8 * u : 8 * u + 8, :]
        end_ref[pl.ds(m, 1), :] = jnp.sum(inner * fine_ref[m], axis=0, keepdims=True)
        return carry

    lax.fori_loop(0, coarse_ref.shape[0], mode, 0)


def front(q_in, k_in, v_in, before, short_filter, decay):
    rows, width = q_in.shape
    modes = decay.shape[0]
    chunks = rows // 8
    coarse = jnp.exp(-decay[:, None, :] * (8.0 * (chunks - 1 - jnp.arange(chunks, dtype=jnp.float32)))[None, :, None])
    fine = jnp.exp(-decay[:, None, :] * (7.0 - jnp.arange(8, dtype=jnp.float32))[None, :, None])
    vmem = pl.BlockSpec(memory_space=pltpu.VMEM)
    return pl.pallas_call(
        front_kernel,
        out_shape=(
            jax.ShapeDtypeStruct((rows, width), jnp.float32),
            jax.ShapeDtypeStruct((rows, width), jnp.float32),
            jax.ShapeDtypeStruct((modes, width), jnp.float32),
        ),
        in_specs=[vmem] * 7,
        out_specs=(vmem, vmem, vmem),
        scratch_shapes=[pltpu.VMEM((3, rows + 8, width), jnp.float32)],
        compiler_params=pltpu.CompilerParams(vmem_limit_bytes=48 * 1024 * 1024),
        cost_estimate=pl.CostEstimate(
            flops=2 * rows * width * (9 + 2 * modes), transcendentals=0, bytes_accessed=rows * width * 14
        ),
    )(q_in, k_in, v_in, before, short_filter, coarse, fine)


def per_device(q_in, k_in, v_in, short_filter, rate, residue, resid, gain):
    rows, width = q_in.shape
    taps = short_filter.shape[1]
    decay = rate.T
    weight = residue.T
    modes = decay.shape[0]
    no_halo = jnp.zeros((3, taps - 1, width), q_in.dtype)
    q_feat, values, ending = front(q_in, k_in, v_in, no_halo, short_filter, decay)
    heads = jnp.concatenate([k_in[:2], v_in[:2]], axis=0).astype(jnp.float32)
    tails = jnp.concatenate([q_in[rows - 2 :], k_in[rows - 2 :], v_in[rows - 2 :]], axis=0).astype(jnp.float32)
    payload = jnp.concatenate([ending, values[:2], heads, tails], axis=0)
    block = min(128, rows)
    blocks = values.reshape(rows // block, block, width)
    offsets = jnp.arange(block, dtype=jnp.int32).astype(jnp.float32)
    grow = jnp.exp(decay[:, None, :] * offsets[None, :, None])
    fade = jnp.exp(-decay[:, None, :] * offsets[None, :, None])
    enter = jnp.exp(-decay[:, None, :] * (offsets[None, :, None] + 1.0))
    zeros = jnp.zeros(decay.shape, jnp.float32)

    def main_step(state, piece):
        running = jnp.cumsum(piece[None, :, :] * grow, axis=1) * fade
        states = running + enter * state[:, None, :]
        return (states[:, -1, :], jnp.sum(states * weight[:, None, :], axis=0))

    def local():
        if rows == block:
            running = jnp.cumsum(values[None, :, :] * grow, axis=1) * fade
            return jnp.sum(running * weight[:, None, :], axis=0)
        return lax.scan(main_step, zeros, blocks)[1].reshape(rows, width)

    incoming, own_tail, outputs = scan_in(payload, modes, short_filter, decay, rows, "ctx", local)
    own_gated = edge_gated(short_filter, heads[0:2], heads[2:4], own_tail[2:4], own_tail[4:6])
    change = own_gated - values[:2]
    q_edge = edge_rows(short_filter[0], q_in[:2].astype(jnp.float32), own_tail[0:2])
    q_feat = jnp.concatenate([q_edge, q_feat[2:]], axis=0)
    grow_one = jnp.exp(decay)
    state = incoming + grow_one * change[0][None, :] + grow_one * grow_one * change[1][None, :]
    spill = change[1] * jnp.sum(weight * grow_one, axis=0)
    times = jnp.arange(rows, dtype=jnp.int32).astype(jnp.float32) + 1.0
    weights = weight * state
    mixed_in = outputs
    for m in range(decay.shape[0]):
        mixed_in = mixed_in + jnp.exp(-decay[m][None, :] * times[:, None]) * weights[m][None, :]
    mixed = mixed_in - jnp.concatenate([spill[None, :], jnp.zeros((rows - 1, width), jnp.float32)], axis=0)
    stream = resid.astype(jnp.float32) + q_feat * mixed
    squares = butterfly_sum(jnp.sum(stream * stream, axis=1), "tp")
    scale = lax.rsqrt(squares / D + 1e-05)
    return (stream * scale[:, None] * gain[None, :]).astype(jnp.bfloat16)


def solution(mesh):
    in_specs = (
        P("ctx", "tp"),
        P("ctx", "tp"),
        P("ctx", "tp"),
        P(None, None, "tp"),
        P("tp", None),
        P("tp", None),
        P("ctx", "tp"),
        P("tp"),
    )
    out_specs = P("ctx", "tp")
    step = jax.shard_map(
        per_device, mesh=mesh, in_specs=in_specs, out_specs=out_specs, check_vma=False
    )
    return step
```

```python
import jax
import jax.numpy as jnp
from jax import lax
from jax.sharding import PartitionSpec as P
from jax.experimental import pallas as pl
from jax.experimental.pallas import tpu as pltpu

D = 8192


def from_behind(block, axis, distance):
    devices = range(lax.axis_size(axis))
    route = [(i - distance, i) for i in devices if i - distance in devices]
    return lax.ppermute(block, axis, route)


def edge_rows(taps, head, tail):
    first = taps[0] * head[0] + taps[1] * tail[1] + taps[2] * tail[0]
    second = taps[0] * head[1] + taps[1] * head[0] + taps[2] * tail[1]
    return jnp.stack([first, second])


def edge_gated(short_filter, head_k, head_v, tail_k, tail_v):
    keys = edge_rows(short_filter[1], head_k, tail_k)
    values = edge_rows(short_filter[2], head_v, tail_v)
    return (keys * values).astype(jnp.bfloat16).astype(jnp.float32)


def scan_in(payload, modes, short_filter, decay, rows, axis, cover):
    count = lax.axis_size(axis)
    radix = min(count, 8)
    got = {shift: from_behind(payload, axis, shift) for shift in range(1, radix + 1) if shift < count}
    covered = cover()
    got, covered = lax.optimization_barrier((got, covered))
    nothing = jnp.zeros_like(payload)
    first_end = jnp.exp(-decay * (rows - 1))
    second_end = jnp.exp(-decay * (rows - 2))

    def block_state(shift):
        piece = got[shift]
        before = got.get(shift + 1, nothing)
        start = modes + 2
        fixed = edge_gated(
            short_filter, piece[start : start + 2], piece[start + 2 : start + 4],
            before[start + 6 : start + 8], before[start + 8 : start + 10],
        )
        change = fixed - piece[modes : modes + 2]
        return piece[:modes] + change[0][None, :] * first_end + change[1][None, :] * second_end

    incoming = jnp.zeros((modes, payload.shape[1]), jnp.float32)
    for shift in range(1, radix):
        incoming = incoming + jnp.exp(-decay * (rows * (shift - 1))) * block_state(shift)
    span = radix - 1
    while span < count - 1:
        incoming = incoming + jnp.exp(-decay * (rows * span)) * from_behind(incoming, axis, span)
        span *= 2
    own_tail = got[1][modes + 6 : modes + 12] if 1 in got else nothing[modes + 6 : modes + 12]
    return incoming, own_tail, covered


def butterfly_sum(value, axis):
    count = lax.axis_size(axis)
    assert count & (count - 1) == 0
    step = 1
    while step < count:
        value = value + lax.ppermute(value, axis, [(i, i ^ step) for i in range(count)])
        step *= 2
    return value


def front_kernel(q_ref, k_ref, v_ref, halo_ref, taps_ref, coarse_ref, fine_ref, qf_ref, g_ref, end_ref, pad_ref):
    rows = q_ref.shape[0]
    lead = pad_ref.shape[1] - rows
    feats = []
    for i, ref in enumerate((q_ref, k_ref, v_ref)):
        pad_ref[i, lead:, :] = ref[...].astype(jnp.float32)
        pad_ref[i, lead - 2 : lead, :] = halo_ref[i].astype(jnp.float32)
        acc = taps_ref[i, 0:1, :] * pad_ref[i, lead:, :]
        for j in (1, 2):
            acc = acc + taps_ref[i, j : j + 1, :] * pad_ref[i, lead - j : lead - j + rows, :]
        feats.append(acc)
    qf_ref[...] = feats[0]
    gated = (feats[1] * feats[2]).astype(jnp.bfloat16).astype(jnp.float32)
    g_ref[...] = gated
    chunks = rows // 8

    def mode(m, carry):
        weights = coarse_ref[m]
        inner = weights[0:1, :] * gated[0:8, :]
        for u in range(1, chunks):
            inner = inner + weights[u : u + 1, :] * gated[8 * u : 8 * u + 8, :]
        end_ref[pl.ds(m, 1), :] = jnp.sum(inner * fine_ref[m], axis=0, keepdims=True)
        return carry

    lax.fori_loop(0, coarse_ref.shape[0], mode, 0)


def front(q_in, k_in, v_in, before, short_filter, decay):
    rows, width = q_in.shape
    modes = decay.shape[0]
    chunks = rows // 8
    coarse = jnp.exp(-decay[:, None, :] * (8.0 * (chunks - 1 - jnp.arange(chunks, dtype=jnp.float32)))[None, :, None])
    fine = jnp.exp(-decay[:, None, :] * (7.0 - jnp.arange(8, dtype=jnp.float32))[None, :, None])
    vmem = pl.BlockSpec(memory_space=pltpu.VMEM)
    return pl.pallas_call(
        front_kernel,
        out_shape=(
            jax.ShapeDtypeStruct((rows, width), jnp.float32),
            jax.ShapeDtypeStruct((rows, width), jnp.float32),
            jax.ShapeDtypeStruct((modes, width), jnp.float32),
        ),
        in_specs=[vmem] * 7,
        out_specs=(vmem, vmem, vmem),
        scratch_shapes=[pltpu.VMEM((3, rows + 8, width), jnp.float32)],
        compiler_params=pltpu.CompilerParams(vmem_limit_bytes=48 * 1024 * 1024),
        cost_estimate=pl.CostEstimate(
            flops=2 * rows * width * (9 + 2 * modes), transcendentals=0, bytes_accessed=rows * width * 14
        ),
    )(q_in, k_in, v_in, before, short_filter, coarse, fine)


def mixer(q_in, k_in, v_in, short_filter, rate, residue, resid, gain):
    rows, width = q_in.shape
    taps = short_filter.shape[1]
    decay = rate.T
    weight = residue.T
    modes = decay.shape[0]
    no_halo = jnp.zeros((3, taps - 1, width), q_in.dtype)
    q_feat, values, ending = front(q_in, k_in, v_in, no_halo, short_filter, decay)
    heads = jnp.concatenate([k_in[:2], v_in[:2]], axis=0).astype(jnp.float32)
    tails = jnp.concatenate([q_in[rows - 2 :], k_in[rows - 2 :], v_in[rows - 2 :]], axis=0).astype(jnp.float32)
    payload = jnp.concatenate([ending, values[:2], heads, tails], axis=0)
    block = min(128, rows)
    blocks = values.reshape(rows // block, block, width)
    offsets = jnp.arange(block, dtype=jnp.int32).astype(jnp.float32)
    grow = jnp.exp(decay[:, None, :] * offsets[None, :, None])
    fade = jnp.exp(-decay[:, None, :] * offsets[None, :, None])
    enter = jnp.exp(-decay[:, None, :] * (offsets[None, :, None] + 1.0))
    zeros = jnp.zeros(decay.shape, jnp.float32)

    def main_step(state, piece):
        running = jnp.cumsum(piece[None, :, :] * grow, axis=1) * fade
        states = running + enter * state[:, None, :]
        return (states[:, -1, :], jnp.sum(states * weight[:, None, :], axis=0))

    def local():
        if rows == block:
            running = jnp.cumsum(values[None, :, :] * grow, axis=1) * fade
            return jnp.sum(running * weight[:, None, :], axis=0)
        return lax.scan(main_step, zeros, blocks)[1].reshape(rows, width)

    incoming, own_tail, outputs = scan_in(payload, modes, short_filter, decay, rows, "ctx", local)
    own_gated = edge_gated(short_filter, heads[0:2], heads[2:4], own_tail[2:4], own_tail[4:6])
    change = own_gated - values[:2]
    q_edge = edge_rows(short_filter[0], q_in[:2].astype(jnp.float32), own_tail[0:2])
    q_feat = jnp.concatenate([q_edge, q_feat[2:]], axis=0)
    grow_one = jnp.exp(decay)
    state = incoming + grow_one * change[0][None, :] + grow_one * grow_one * change[1][None, :]
    spill = change[1] * jnp.sum(weight * grow_one, axis=0)
    times = jnp.arange(rows, dtype=jnp.int32).astype(jnp.float32) + 1.0
    weights = weight * state
    mixed_in = outputs
    for m in range(decay.shape[0]):
        mixed_in = mixed_in + jnp.exp(-decay[m][None, :] * times[:, None]) * weights[m][None, :]
    mixed = mixed_in - jnp.concatenate([spill[None, :], jnp.zeros((rows - 1, width), jnp.float32)], axis=0)
    stream = resid.astype(jnp.float32) + q_feat * mixed
    squares = butterfly_sum(jnp.sum(stream * stream, axis=1), "tp")
    scale = lax.rsqrt(squares / D + 1e-05)
    return (stream * scale[:, None] * gain[None, :]).astype(jnp.bfloat16)


def solution(mesh):
    in_specs = (
        P("ctx", "tp"),
        P("ctx", "tp"),
        P("ctx", "tp"),
        P(None, None, "tp"),
        P("tp", None),
        P("tp", None),
        P("ctx", "tp"),
        P("tp"),
    )
    out_specs = P("ctx", "tp")
    return jax.shard_map(mixer, mesh=mesh, in_specs=in_specs, out_specs=out_specs, check_vma=False)
```

```python
import jax
import jax.numpy as jnp
from jax import lax
from jax.sharding import PartitionSpec as P
from jax.experimental import pallas as pl
from jax.experimental.pallas import tpu as pltpu

D = 8192


def from_behind(block, axis, distance):
    devices = range(lax.axis_size(axis))
    route = [(i - distance, i) for i in devices if i - distance in devices]
    return lax.ppermute(block, axis, route)


def scan_in(ending, rate, rows, axis, cover):
    count = lax.axis_size(axis)
    radix = min(count, 8)
    arrived = [from_behind(ending, axis, shift) for shift in range(1, radix)]
    arrived, covered = lax.optimization_barrier((arrived, cover()))
    incoming = jnp.zeros_like(ending)
    for shift in range(1, radix):
        incoming = incoming + jnp.exp(-rate * (rows * (shift - 1))) * arrived[shift - 1]
    span = radix - 1
    while span < count - 1:
        incoming = incoming + jnp.exp(-rate * (rows * span)) * from_behind(incoming, axis, span)
        span *= 2
    return incoming, covered


def butterfly_sum(value, axis):
    count = lax.axis_size(axis)
    assert count & (count - 1) == 0
    step = 1
    while step < count:
        value = value + lax.ppermute(value, axis, [(i, i ^ step) for i in range(count)])
        step *= 2
    return value


def front_kernel(q_ref, k_ref, v_ref, halo_ref, taps_ref, coarse_ref, fine_ref, qf_ref, g_ref, end_ref, pad_ref):
    rows = q_ref.shape[0]
    lead = pad_ref.shape[1] - rows
    feats = []
    for i, ref in enumerate((q_ref, k_ref, v_ref)):
        pad_ref[i, lead:, :] = ref[...].astype(jnp.float32)
        pad_ref[i, lead - 2 : lead, :] = halo_ref[i].astype(jnp.float32)
        acc = taps_ref[i, 0:1, :] * pad_ref[i, lead:, :]
        for j in (1, 2):
            acc = acc + taps_ref[i, j : j + 1, :] * pad_ref[i, lead - j : lead - j + rows, :]
        feats.append(acc)
    qf_ref[...] = feats[0]
    gated = (feats[1] * feats[2]).astype(jnp.bfloat16).astype(jnp.float32)
    g_ref[...] = gated
    chunks = rows // 8

    def mode(m, carry):
        weights = coarse_ref[m]
        inner = weights[0:1, :] * gated[0:8, :]
        for u in range(1, chunks):
            inner = inner + weights[u : u + 1, :] * gated[8 * u : 8 * u + 8, :]
        end_ref[pl.ds(m, 1), :] = jnp.sum(inner * fine_ref[m], axis=0, keepdims=True)
        return carry

    lax.fori_loop(0, coarse_ref.shape[0], mode, 0)


def front(q_in, k_in, v_in, before, short_filter, decay):
    rows, width = q_in.shape
    modes = decay.shape[0]
    chunks = rows // 8
    coarse = jnp.exp(-decay[:, None, :] * (8.0 * (chunks - 1 - jnp.arange(chunks, dtype=jnp.float32)))[None, :, None])
    fine = jnp.exp(-decay[:, None, :] * (7.0 - jnp.arange(8, dtype=jnp.float32))[None, :, None])
    vmem = pl.BlockSpec(memory_space=pltpu.VMEM)
    return pl.pallas_call(
        front_kernel,
        out_shape=(
            jax.ShapeDtypeStruct((rows, width), jnp.float32),
            jax.ShapeDtypeStruct((rows, width), jnp.float32),
            jax.ShapeDtypeStruct((modes, width), jnp.float32),
        ),
        in_specs=[vmem] * 7,
        out_specs=(vmem, vmem, vmem),
        scratch_shapes=[pltpu.VMEM((3, rows + 8, width), jnp.float32)],
        compiler_params=pltpu.CompilerParams(vmem_limit_bytes=48 * 1024 * 1024),
        cost_estimate=pl.CostEstimate(
            flops=2 * rows * width * (9 + 2 * modes), transcendentals=0, bytes_accessed=rows * width * 14
        ),
    )(q_in, k_in, v_in, before, short_filter, coarse, fine)


def per_device(q_in, k_in, v_in, short_filter, rate, residue, resid, gain):
    rows, width = q_in.shape
    taps = short_filter.shape[1]
    stacked = jnp.stack([q_in, k_in, v_in])
    tail = stacked[:, rows - (taps - 1) :, :]
    before = from_behind(tail, "ctx", 1)
    decay = rate.T
    weight = residue.T
    q_feat, values, ending = front(q_in, k_in, v_in, before, short_filter, decay)
    block = min(128, rows)
    blocks = values.reshape(rows // block, block, width)
    offsets = jnp.arange(block, dtype=jnp.int32).astype(jnp.float32)
    grow = jnp.exp(decay[:, None, :] * offsets[None, :, None])
    fade = jnp.exp(-decay[:, None, :] * offsets[None, :, None])
    enter = jnp.exp(-decay[:, None, :] * (offsets[None, :, None] + 1.0))
    zeros = jnp.zeros(decay.shape, jnp.float32)

    def main_step(state, piece):
        running = jnp.cumsum(piece[None, :, :] * grow, axis=1) * fade
        states = running + enter * state[:, None, :]
        return (states[:, -1, :], jnp.sum(states * weight[:, None, :], axis=0))

    def local():
        if rows == block:
            running = jnp.cumsum(values[None, :, :] * grow, axis=1) * fade
            return jnp.sum(running * weight[:, None, :], axis=0)
        return lax.scan(main_step, zeros, blocks)[1].reshape(rows, width)

    incoming, outputs = scan_in(ending, decay, rows, "ctx", local)
    times = jnp.arange(rows, dtype=jnp.int32).astype(jnp.float32) + 1.0
    weights = weight * incoming
    mixed_in = outputs
    if rows % 8 == 0:
        coarse_t = jnp.arange(0, rows, 8, dtype=jnp.int32).astype(jnp.float32)
        fine_t = jnp.arange(8, dtype=jnp.int32).astype(jnp.float32) + 1.0
        far = jnp.exp(-decay[:, None, :] * coarse_t[None, :, None]) * weights[:, None, :]
        near = jnp.exp(-decay[:, None, :] * fine_t[None, :, None])
        for m in range(decay.shape[0]):
            mixed_in = mixed_in + (far[m][:, None, :] * near[m][None, :, :]).reshape(rows, width)
    else:
        for m in range(decay.shape[0]):
            mixed_in = mixed_in + jnp.exp(-decay[m][None, :] * times[:, None]) * weights[m][None, :]
    mixed = mixed_in
    stream = resid.astype(jnp.float32) + q_feat * mixed
    squares = butterfly_sum(jnp.sum(stream * stream, axis=1), "tp")
    scale = lax.rsqrt(squares / D + 1e-05)
    return (stream * scale[:, None] * gain[None, :]).astype(jnp.bfloat16)


def solution(mesh):
    in_specs = (
        P("ctx", "tp"),
        P("ctx", "tp"),
        P("ctx", "tp"),
        P(None, None, "tp"),
        P("tp", None),
        P("tp", None),
        P("ctx", "tp"),
        P("tp"),
    )
    out_specs = P("ctx", "tp")
    step = jax.shard_map(
        per_device, mesh=mesh, in_specs=in_specs, out_specs=out_specs, check_vma=False
    )
    return step
```

```python
import jax
import jax.numpy as jnp
from jax import lax
from jax.sharding import PartitionSpec as P
from jax.experimental import pallas as pl
from jax.experimental.pallas import tpu as pltpu

D = 8192


def from_behind(block, axis, distance):
    devices = range(lax.axis_size(axis))
    route = [(i - distance, i) for i in devices if i - distance in devices]
    return lax.ppermute(block, axis, route)


def scan_in(ending, rate, rows, axis, cover):
    count = lax.axis_size(axis)
    radix = min(count, 8)
    arrived = [from_behind(ending, axis, shift) for shift in range(1, radix)]
    arrived, covered = lax.optimization_barrier((arrived, cover()))
    incoming = jnp.zeros_like(ending)
    for shift in range(1, radix):
        incoming = incoming + jnp.exp(-rate * (rows * (shift - 1))) * arrived[shift - 1]
    span = radix - 1
    while span < count - 1:
        incoming = incoming + jnp.exp(-rate * (rows * span)) * from_behind(incoming, axis, span)
        span *= 2
    return incoming, covered


def butterfly_sum(value, axis):
    count = lax.axis_size(axis)
    assert count & (count - 1) == 0
    step = 1
    while step < count:
        value = value + lax.ppermute(value, axis, [(i, i ^ step) for i in range(count)])
        step *= 2
    return value


def front_kernel(q_ref, k_ref, v_ref, halo_ref, taps_ref, coarse_ref, fine_ref, qf_ref, g_ref, end_ref, pad_ref):
    rows = q_ref.shape[0]
    lead = pad_ref.shape[1] - rows
    feats = []
    for i, ref in enumerate((q_ref, k_ref, v_ref)):
        pad_ref[i, lead:, :] = ref[...].astype(jnp.float32)
        pad_ref[i, lead - 2 : lead, :] = halo_ref[i].astype(jnp.float32)
        acc = taps_ref[i, 0:1, :] * pad_ref[i, lead:, :]
        for j in (1, 2):
            acc = acc + taps_ref[i, j : j + 1, :] * pad_ref[i, lead - j : lead - j + rows, :]
        feats.append(acc)
    qf_ref[...] = feats[0]
    gated = (feats[1] * feats[2]).astype(jnp.bfloat16).astype(jnp.float32)
    g_ref[...] = gated
    chunks = rows // 8

    def mode(m, carry):
        weights = coarse_ref[m]
        inner = weights[0:1, :] * gated[0:8, :]
        for u in range(1, chunks):
            inner = inner + weights[u : u + 1, :] * gated[8 * u : 8 * u + 8, :]
        end_ref[pl.ds(m, 1), :] = jnp.sum(inner * fine_ref[m], axis=0, keepdims=True)
        return carry

    lax.fori_loop(0, coarse_ref.shape[0], mode, 0)


def front(q_in, k_in, v_in, before, short_filter, decay):
    rows, width = q_in.shape
    modes = decay.shape[0]
    chunks = rows // 8
    coarse = jnp.exp(-decay[:, None, :] * (8.0 * (chunks - 1 - jnp.arange(chunks, dtype=jnp.float32)))[None, :, None])
    fine = jnp.exp(-decay[:, None, :] * (7.0 - jnp.arange(8, dtype=jnp.float32))[None, :, None])
    vmem = pl.BlockSpec(memory_space=pltpu.VMEM)
    return pl.pallas_call(
        front_kernel,
        out_shape=(
            jax.ShapeDtypeStruct((rows, width), jnp.float32),
            jax.ShapeDtypeStruct((rows, width), jnp.float32),
            jax.ShapeDtypeStruct((modes, width), jnp.float32),
        ),
        in_specs=[vmem] * 7,
        out_specs=(vmem, vmem, vmem),
        scratch_shapes=[pltpu.VMEM((3, rows + 8, width), jnp.float32)],
        compiler_params=pltpu.CompilerParams(vmem_limit_bytes=48 * 1024 * 1024),
        cost_estimate=pl.CostEstimate(
            flops=2 * rows * width * (9 + 2 * modes), transcendentals=0, bytes_accessed=rows * width * 14
        ),
    )(q_in, k_in, v_in, before, short_filter, coarse, fine)


def per_device(q_in, k_in, v_in, short_filter, rate, residue, resid, gain):
    rows, width = q_in.shape
    taps = short_filter.shape[1]
    stacked = jnp.stack([q_in, k_in, v_in])
    tail = stacked[:, rows - (taps - 1) :, :]
    before = from_behind(tail, "ctx", 1)
    decay = rate.T
    weight = residue.T
    q_feat, values, ending = front(q_in, k_in, v_in, before, short_filter, decay)
    block = min(128, rows)
    blocks = values.reshape(rows // block, block, width)
    offsets = jnp.arange(block, dtype=jnp.int32).astype(jnp.float32)
    grow = jnp.exp(decay[:, None, :] * offsets[None, :, None])
    fade = jnp.exp(-decay[:, None, :] * offsets[None, :, None])
    enter = jnp.exp(-decay[:, None, :] * (offsets[None, :, None] + 1.0))
    zeros = jnp.zeros(decay.shape, jnp.float32)

    def main_step(state, piece):
        running = jnp.cumsum(piece[None, :, :] * grow, axis=1) * fade
        states = running + enter * state[:, None, :]
        return (states[:, -1, :], jnp.sum(states * weight[:, None, :], axis=0))

    def local():
        return local_part(), resid.astype(jnp.float32)

    def local_part():
        if rows == block:
            running = jnp.cumsum(values[None, :, :] * grow, axis=1) * fade
            return jnp.sum(running * weight[:, None, :], axis=0)
        return lax.scan(main_step, zeros, blocks)[1].reshape(rows, width)

    incoming, (outputs, resid_f32) = scan_in(ending, decay, rows, "ctx", local)
    times = jnp.arange(rows, dtype=jnp.int32).astype(jnp.float32) + 1.0
    weights = weight * incoming
    mixed_in = outputs
    if rows % 8 == 0:
        coarse_t = jnp.arange(0, rows, 8, dtype=jnp.int32).astype(jnp.float32)
        fine_t = jnp.arange(8, dtype=jnp.int32).astype(jnp.float32) + 1.0
        far = jnp.exp(-decay[:, None, :] * coarse_t[None, :, None]) * weights[:, None, :]
        near = jnp.exp(-decay[:, None, :] * fine_t[None, :, None])
        for m in range(decay.shape[0]):
            mixed_in = mixed_in + (far[m][:, None, :] * near[m][None, :, :]).reshape(rows, width)
    else:
        for m in range(decay.shape[0]):
            mixed_in = mixed_in + jnp.exp(-decay[m][None, :] * times[:, None]) * weights[m][None, :]
    mixed = mixed_in
    stream = resid_f32 + q_feat * mixed
    squares = butterfly_sum(jnp.sum(stream * stream, axis=1), "tp")
    scale = lax.rsqrt(squares / D + 1e-05)
    return (stream * scale[:, None] * gain[None, :]).astype(jnp.bfloat16)


def solution(mesh):
    in_specs = (
        P("ctx", "tp"),
        P("ctx", "tp"),
        P("ctx", "tp"),
        P(None, None, "tp"),
        P("tp", None),
        P("tp", None),
        P("ctx", "tp"),
        P("tp"),
    )
    out_specs = P("ctx", "tp")
    step = jax.shard_map(
        per_device, mesh=mesh, in_specs=in_specs, out_specs=out_specs, check_vma=False
    )
    return step
```

```python
import jax
import jax.numpy as jnp
from jax import lax
from jax.sharding import PartitionSpec as P
from jax.experimental import pallas as pl
from jax.experimental.pallas import tpu as pltpu

D = 8192


def from_behind(block, axis, distance):
    devices = range(lax.axis_size(axis))
    route = [(i - distance, i) for i in devices if i - distance in devices]
    return lax.ppermute(block, axis, route)


def scan_in(ending, rate, rows, axis, cover):
    count = lax.axis_size(axis)
    radix = min(count, 8)
    arrived = [from_behind(ending, axis, shift) for shift in range(1, radix)]
    arrived, covered = lax.optimization_barrier((arrived, cover()))
    incoming = jnp.zeros_like(ending)
    for shift in range(1, radix):
        incoming = incoming + jnp.exp(-rate * (rows * (shift - 1))) * arrived[shift - 1]
    span = radix - 1
    while span < count - 1:
        incoming = incoming + jnp.exp(-rate * (rows * span)) * from_behind(incoming, axis, span)
        span *= 2
    return incoming, covered


def butterfly_sum(value, axis):
    count = lax.axis_size(axis)
    assert count & (count - 1) == 0
    step = 1
    while step < count:
        value = value + lax.ppermute(value, axis, [(i, i ^ step) for i in range(count)])
        step *= 2
    return value


def front_kernel(q_ref, k_ref, v_ref, halo_ref, taps_ref, decay_ref, qf_ref, g_ref, end_ref, pad_ref):
    rows = q_ref.shape[0]
    lead = pad_ref.shape[1] - rows
    feats = []
    for i, ref in enumerate((q_ref, k_ref, v_ref)):
        pad_ref[i, lead:, :] = ref[...].astype(jnp.float32)
        pad_ref[i, lead - 2 : lead, :] = halo_ref[i].astype(jnp.float32)
        acc = taps_ref[i, 0:1, :] * pad_ref[i, lead:, :]
        for j in (1, 2):
            acc = acc + taps_ref[i, j : j + 1, :] * pad_ref[i, lead - j : lead - j + rows, :]
        feats.append(acc)
    qf_ref[...] = feats[0]
    gated = (feats[1] * feats[2]).astype(jnp.bfloat16).astype(jnp.float32)
    g_ref[...] = gated
    chunks = rows // 8

    far = (8.0 * (chunks - 1) - 8.0 * lax.broadcasted_iota(jnp.int32, (chunks, 1), 0).astype(jnp.float32))
    near = 7.0 - lax.broadcasted_iota(jnp.int32, (8, 1), 0).astype(jnp.float32)

    def mode(m, carry):
        rate_row = decay_ref[pl.ds(m, 1), :]
        weights = jnp.exp(-rate_row * far)
        fine = jnp.exp(-rate_row * near)
        inner = weights[0:1, :] * gated[0:8, :]
        for u in range(1, chunks):
            inner = inner + weights[u : u + 1, :] * gated[8 * u : 8 * u + 8, :]
        end_ref[pl.ds(m, 1), :] = jnp.sum(inner * fine, axis=0, keepdims=True)
        return carry

    lax.fori_loop(0, decay_ref.shape[0], mode, 0)


def front(q_in, k_in, v_in, before, short_filter, decay):
    rows, width = q_in.shape
    modes = decay.shape[0]
    chunks = rows // 8
    vmem = pl.BlockSpec(memory_space=pltpu.VMEM)
    return pl.pallas_call(
        front_kernel,
        out_shape=(
            jax.ShapeDtypeStruct((rows, width), jnp.float32),
            jax.ShapeDtypeStruct((rows, width), jnp.float32),
            jax.ShapeDtypeStruct((modes, width), jnp.float32),
        ),
        in_specs=[vmem] * 6,
        out_specs=(vmem, vmem, vmem),
        scratch_shapes=[pltpu.VMEM((3, rows + 8, width), jnp.float32)],
        compiler_params=pltpu.CompilerParams(vmem_limit_bytes=48 * 1024 * 1024),
        cost_estimate=pl.CostEstimate(
            flops=2 * rows * width * (9 + 2 * modes), transcendentals=0, bytes_accessed=rows * width * 14
        ),
    )(q_in, k_in, v_in, before, short_filter, decay)


def per_device(q_in, k_in, v_in, short_filter, rate, residue, resid, gain):
    rows, width = q_in.shape
    taps = short_filter.shape[1]
    stacked = jnp.stack([q_in, k_in, v_in])
    tail = stacked[:, rows - (taps - 1) :, :]
    before = from_behind(tail, "ctx", 1)
    decay = rate.T
    weight = residue.T
    q_feat, values, ending = front(q_in, k_in, v_in, before, short_filter, decay)
    block = min(128, rows)
    blocks = values.reshape(rows // block, block, width)
    offsets = jnp.arange(block, dtype=jnp.int32).astype(jnp.float32)
    grow = jnp.exp(decay[:, None, :] * offsets[None, :, None])
    fade = jnp.exp(-decay[:, None, :] * offsets[None, :, None])
    enter = jnp.exp(-decay[:, None, :] * (offsets[None, :, None] + 1.0))
    zeros = jnp.zeros(decay.shape, jnp.float32)

    def main_step(state, piece):
        running = jnp.cumsum(piece[None, :, :] * grow, axis=1) * fade
        states = running + enter * state[:, None, :]
        return (states[:, -1, :], jnp.sum(states * weight[:, None, :], axis=0))

    def local():
        return local_part(), resid.astype(jnp.float32)

    def local_part():
        if rows == block:
            running = jnp.cumsum(values[None, :, :] * grow, axis=1) * fade
            return jnp.sum(running * weight[:, None, :], axis=0)
        return lax.scan(main_step, zeros, blocks)[1].reshape(rows, width)

    incoming, (outputs, resid_f32) = scan_in(ending, decay, rows, "ctx", local)
    times = jnp.arange(rows, dtype=jnp.int32).astype(jnp.float32) + 1.0
    weights = weight * incoming
    mixed_in = outputs
    if rows % 8 == 0:
        coarse_t = jnp.arange(0, rows, 8, dtype=jnp.int32).astype(jnp.float32)
        fine_t = jnp.arange(8, dtype=jnp.int32).astype(jnp.float32) + 1.0
        far = jnp.exp(-decay[:, None, :] * coarse_t[None, :, None]) * weights[:, None, :]
        near = jnp.exp(-decay[:, None, :] * fine_t[None, :, None])
        for m in range(decay.shape[0]):
            mixed_in = mixed_in + (far[m][:, None, :] * near[m][None, :, :]).reshape(rows, width)
    else:
        for m in range(decay.shape[0]):
            mixed_in = mixed_in + jnp.exp(-decay[m][None, :] * times[:, None]) * weights[m][None, :]
    mixed = mixed_in
    stream = resid_f32 + q_feat * mixed
    squares = butterfly_sum(jnp.sum(stream * stream, axis=1), "tp")
    scale = lax.rsqrt(squares / D + 1e-05)
    return (stream * scale[:, None] * gain[None, :]).astype(jnp.bfloat16)


def solution(mesh):
    in_specs = (
        P("ctx", "tp"),
        P("ctx", "tp"),
        P("ctx", "tp"),
        P(None, None, "tp"),
        P("tp", None),
        P("tp", None),
        P("ctx", "tp"),
        P("tp"),
    )
    out_specs = P("ctx", "tp")
    step = jax.shard_map(
        per_device, mesh=mesh, in_specs=in_specs, out_specs=out_specs, check_vma=False
    )
    return step
```
